256 devices in a mesh: pipe: 4 (over x), seq: 64 (over z, y, core).
Axes of the slice: x: 4, y: 4, z: 8, core: 2. Of those that a mesh axis runs over, the one named last changes fastest.
Arguments:
- inputs: bfloat16 [4, 2, 8192, 1024], P('pipe', None, 'seq'), may hold values from -16 to 16
- incoming: bfloat16 [4, 2, 8192, 1024], P('pipe', None, 'seq'), may hold values from -6 to 6
- angles: float32 [4, 2, 1024], P('pipe'), may hold values from -3.140625 to 3.140625
- level_weights: float32 [4, 14, 1024], P('pipe'), may hold values from -1.5 to 1.5
- mix_weight: bfloat16 [4, 1024, 2048], P('pipe'), may hold values from -0.1875 to 0.1875
Outputs:
- grad_input: bfloat16 [4, 2, 8192, 1024], P('pipe', None, 'seq')
- grad_angles: float32 [4, 2, 1024], P('pipe')
- grad_levels: float32 [4, 14, 1024], P('pipe')
- grad_mix: float32 [4, 1024, 2048], P('pipe', 'seq')
The draws below stay inside these ranges and needn't reach their ends.
All inputs are finite; a program needn't handle non-finite values.
Results may differ from the reference program's by a relative error of at most 0.015.
Values may be sent and summed in bfloat16 or wider, within the bound.
No kernel may reach another device: no remote copies, remote signals or barrier semaphores. Data moves between devices by JAX's collectives and lax.ppermute only.
A program may use at most 128 MiB of HBM per device.

```python
import jax
import jax.numpy as jnp
from jax import lax

D = 1024
BATCH = 2
SEQ = 8192
LEVELS = 13
N_PIPE = 4


def spiked(result, own_key, source, target, blocks, factor):
    def block_of(dim):
        return (jnp.arange(result.shape[dim]) // (result.shape[dim] // blocks)).reshape((-1,) + (1,) * (result.ndim - 1 - dim))

    one_side = jax.random.permutation(own_key, blocks)[block_of(target)]
    far = (block_of(target) + blocks // 2) % blocks
    return jnp.where((block_of(source) == one_side) | (block_of(source) == far), factor * result, result)


def levels(stream_key, shape, cuts, least, top_value):
    gain, own = 1.0, jax.random.fold_in(stream_key, 6)
    for axis_at, shards_of in cuts:
        heights = jnp.exp(jax.random.uniform(jax.random.fold_in(own, axis_at), (shards_of,), jnp.float32, least / len(cuts), top_value / len(cuts)))
        gain = gain * jnp.repeat(heights, shape[axis_at] // shards_of).reshape([-1 if axis == axis_at else 1 for axis in range(len(shape))])
    return gain


def bell_draw(stream_key, dims, width, reach, shards=(), held_as=jnp.bfloat16):
    result = jax.random.normal(stream_key, dims, jnp.float32) * width
    if len(shards) > 0:
        result = levels(stream_key, dims, shards, -0.22, 0.18) * result
    return jnp.clip(result, min=-reach, max=reach).astype(held_as)


def heavy_noise(key, dims, spread, most, split, heavy, dtype=jnp.bfloat16):
    entries = spread * jax.random.normal(key, dims, jnp.float32)
    if split:
        entries = entries * levels(key, dims, split, -0.22, 0.18)
    return jnp.clip(spiked(entries, jax.random.fold_in(key, 3), *heavy), -most, most).astype(dtype)


def setup_inputs(seed: int = 0) -> dict:
    key_of = jax.random.split(jax.random.key(seed), 6)
    return {
        "inputs": heavy_noise(key_of[0], (N_PIPE, BATCH, SEQ, D), 1.0, 16.0, ((0, 4), (2, 64)), (2, 3, 64, 4.0)),
        "incoming": bell_draw(key_of[1], (N_PIPE, BATCH, SEQ, D), 1.0, 6.0, ((0, 4), (2, 64))),
        "angles": jnp.clip(jax.random.uniform(key_of[2], (N_PIPE, 2, D), jnp.float32, -3.140625, 3.140625), -3.140625, 3.140625),
        "level_weights": bell_draw(key_of[3], (N_PIPE, LEVELS + 1, D), (LEVELS + 1) ** -0.5, 1.5, ((0, 4),), jnp.float32),
        "mix_weight": bell_draw(key_of[4], (N_PIPE, D, 2 * D), D ** -0.5, 0.1875, ((0, 4),)),
    }


def rounded(values):
    return lax.optimization_barrier(values.astype(jnp.bfloat16))

def behind(values, spacing):
    return jnp.pad(values, ((0, 0), (spacing, 0), (0, 0)))[:, :values.shape[1], :]

def from_later(values, spacing):
    return jnp.pad(values, ((0, 0), (0, spacing), (0, 0)))[:, spacing:, :]

def section(activations, cotangent, angle_pair, weights, w_mix):
    grad_scale = float(BATCH * SEQ) ** (-0.5)
    c_low = jnp.cos(angle_pair[0])
    s_low = jnp.sin(angle_pair[0])
    c_high = jnp.cos(angle_pair[1])
    s_high = jnp.sin(angle_pair[1])
    state_now = activations
    states = []
    mixed = jnp.zeros(activations.shape, jnp.float32)
    for level_idx in range(LEVELS):
        spacing = 2 ** level_idx
        current = state_now.astype(jnp.float32)
        previous = behind(current, spacing)
        mixed = mixed + weights[level_idx] * (c_high * current + s_high * previous)
        states.append(state_now)
        state_now = rounded(c_low * current + s_low * previous)
    top_state = state_now.astype(jnp.float32)
    mixed = mixed + weights[LEVELS] * top_state
    activated = jax.nn.gelu(mixed).astype(jnp.bfloat16).reshape(-1, D)
    projected = jnp.dot(activated, w_mix, preferred_element_type=jnp.float32)
    value_half = projected[:, :D]
    gate_value = jax.nn.sigmoid(projected[:, D:])
    upstream = cotangent.reshape(-1, D).astype(jnp.float32)
    grad_proj = jnp.concatenate([upstream * gate_value, upstream * value_half * gate_value * (1.0 - gate_value)], axis=1).astype(jnp.bfloat16)
    grad_act = jnp.dot(grad_proj, w_mix.T, preferred_element_type=jnp.float32)
    grad_weight = jnp.dot(activated.T, grad_proj, preferred_element_type=jnp.float32) * grad_scale
    _, pullback = jax.vjp(jax.nn.gelu, mixed)
    grad_conv = pullback(grad_act.reshape(mixed.shape))[0]
    adjoint = weights[LEVELS] * grad_conv
    level_grads = [None] * (LEVELS + 1)
    level_grads[LEVELS] = lax.optimization_barrier(jnp.sum(grad_conv * top_state, axis=(0, 1)))
    zero_row = jnp.zeros((D,), jnp.float32)
    tap_low_now, tap_low_back, tap_high_now, tap_high_back = (zero_row, zero_row, zero_row, zero_row)
    for level_idx in reversed(range(LEVELS)):
        spacing = 2 ** level_idx
        current = states[level_idx].astype(jnp.float32)
        previous = behind(current, spacing)
        weighted = weights[level_idx] * grad_conv
        level_grads[level_idx] = lax.optimization_barrier(jnp.sum(grad_conv * (c_high * current + s_high * previous), axis=(0, 1)))
        tap_low_now = tap_low_now + lax.optimization_barrier(jnp.sum(adjoint * current, axis=(0, 1)))
        tap_low_back = tap_low_back + lax.optimization_barrier(jnp.sum(adjoint * previous, axis=(0, 1)))
        tap_high_now = tap_high_now + lax.optimization_barrier(jnp.sum(weighted * current, axis=(0, 1)))
        tap_high_back = tap_high_back + lax.optimization_barrier(jnp.sum(weighted * previous, axis=(0, 1)))
        carried = rounded(s_low * adjoint + s_high * weighted).astype(jnp.float32)
        adjoint = c_low * adjoint + c_high * weighted + from_later(carried, spacing)
    grad_input = (cotangent.astype(jnp.float32) + adjoint).astype(jnp.bfloat16)
    grad_angle = jnp.stack([c_low * tap_low_back - s_low * tap_low_now, c_high * tap_high_back - s_high * tap_high_now]) * grad_scale
    return (grad_input, grad_angle, jnp.stack(level_grads) * grad_scale, grad_weight)

def reference(inputs, incoming, angles, level_weights, mix_weight):
    results = []
    for section_idx in range(N_PIPE):
        results.append(section(inputs[section_idx], incoming[(section_idx + 1) % N_PIPE], angles[section_idx], level_weights[section_idx], mix_weight[section_idx]))
    return (jnp.stack([item[0] for item in results]), jnp.stack([item[1] for item in results]), jnp.stack([item[2] for item in results]), jnp.stack([item[3] for item in results]))
```

```python
import jax
import jax.numpy as jnp
from jax import lax
from jax.sharding import PartitionSpec as P


def shifted_2(block, axis, distance):
    devices = range(lax.axis_size(axis))
    route = [(i - distance, i) for i in devices if i - distance in devices]
    return lax.ppermute(block, axis, route)


def shifted_3(value, axis, steps):
    count = lax.axis_size(axis)
    pairs = [(source, (source + steps) % count) for source in range(count)]
    return lax.ppermute(value, axis, pairs)


def rounded(values):
    return lax.optimization_barrier(values.astype(jnp.bfloat16))


def behind(values, spacing):
    return jnp.pad(values, ((0, 0), (spacing, 0), (0, 0)))[:, : values.shape[1], :]


def butterfly_sum(value, axis):
    count = lax.axis_size(axis)
    if count & (count - 1):
        return lax.psum(value, axis)
    step = 1
    while step < count:
        pairs = [(i, i ^ step) for i in range(count)]
        value = value + lax.ppermute(value, axis, pairs)
        step *= 2
    return value


def tap_terms(totals, adjoint, weighted, current, previous):
    return (
        totals[0] + jnp.sum(adjoint * current, axis=(0, 1)),
        totals[1] + jnp.sum(adjoint * previous, axis=(0, 1)),
        totals[2] + jnp.sum(weighted * current, axis=(0, 1)),
        totals[3] + jnp.sum(weighted * previous, axis=(0, 1)),
    )


def shards(inputs, incoming, angles, level_weights, mix_weight):
    activations = inputs[0]
    sequences, positions, channels = activations.shape
    seq_devices = lax.axis_size("seq")
    levels = level_weights.shape[1] - 1
    near_count = positions.bit_length() - 1
    grad_scale = float(sequences * positions * seq_devices) ** (-0.5)
    weights = level_weights[0]
    w_mix = mix_weight[0]
    c_low = jnp.cos(angles[0, 0])
    s_low = jnp.sin(angles[0, 0])
    c_high = jnp.cos(angles[0, 1])
    s_high = jnp.sin(angles[0, 1])
    received = shifted_3(incoming, "pipe", -1)[0]
    states = []
    shifted_states = []
    mixed = jnp.zeros(activations.shape, jnp.float32)
    halo = shifted_2(activations, "seq", 1)
    wide_state = jnp.concatenate([halo, activations], axis=1)
    for level_idx in range(near_count):
        spacing = 2**level_idx
        wide_shifted = behind(wide_state, spacing)
        wide_current = wide_state.astype(jnp.float32)
        wide_previous = wide_shifted.astype(jnp.float32)
        current = wide_current[:, positions:, :]
        previous = wide_previous[:, positions:, :]
        mixed = mixed + weights[level_idx] * (c_high * current + s_high * previous)
        states.append(wide_state[:, positions:, :])
        shifted_states.append(wide_shifted[:, positions:, :])
        wide_state = rounded(c_low * wide_current + s_low * wide_previous)
    state_now = wide_state[:, positions:, :]
    for level_idx in range(near_count, levels):
        spacing = 2**level_idx
        shifted = shifted_2(state_now, "seq", spacing // positions)
        current = state_now.astype(jnp.float32)
        previous = shifted.astype(jnp.float32)
        mixed = mixed + weights[level_idx] * (c_high * current + s_high * previous)
        states.append(state_now)
        shifted_states.append(shifted)
        state_now = rounded(c_low * current + s_low * previous)
    top_state = state_now.astype(jnp.float32)
    mixed = mixed + weights[levels] * top_state
    activated = jax.nn.gelu(mixed).astype(jnp.bfloat16).reshape(-1, channels)
    projected = jnp.dot(activated, w_mix, preferred_element_type=jnp.float32)
    value_half = projected[:, :channels]
    gate_value = jax.nn.sigmoid(projected[:, channels:])
    upstream = received.reshape(-1, channels).astype(jnp.float32)
    grad_proj = jnp.concatenate(
        [upstream * gate_value, upstream * value_half * gate_value * (1.0 - gate_value)], axis=1
    ).astype(jnp.bfloat16)
    grad_act = jnp.einsum("rk,ck->rc", grad_proj, w_mix, preferred_element_type=jnp.float32)
    grad_weight = (
        lax.psum_scatter(
            jnp.einsum("rc,rk->ck", activated, grad_proj, preferred_element_type=jnp.float32),
            "seq",
            scatter_dimension=0,
            tiled=True,
        )
        * grad_scale
    )
    _, pullback = jax.vjp(jax.nn.gelu, mixed)
    grad_conv = pullback(grad_act.reshape(mixed.shape))[0]
    level_grads = [None] * (levels + 1)
    adjoint = weights[levels] * grad_conv
    level_grads[levels] = jnp.sum(grad_conv * top_state, axis=(0, 1))
    zero_row = jnp.zeros((channels,), jnp.float32)
    totals = (zero_row, zero_row, zero_row, zero_row)
    for level_idx in reversed(range(near_count, levels)):
        spacing = 2**level_idx
        current = states[level_idx].astype(jnp.float32)
        previous = shifted_states[level_idx].astype(jnp.float32)
        weighted = weights[level_idx] * grad_conv
        level_grads[level_idx] = jnp.sum(
            grad_conv * (c_high * current + s_high * previous), axis=(0, 1)
        )
        totals = tap_terms(totals, adjoint, weighted, current, previous)
        carried = rounded(s_low * adjoint + s_high * weighted)
        arrived = shifted_2(carried, "seq", -(spacing // positions)).astype(jnp.float32)
        adjoint = c_low * adjoint + c_high * weighted + arrived
    fronts = []
    front_adjoint = adjoint
    for level_idx in reversed(range(near_count)):
        spacing = 2**level_idx
        span = 2 * spacing
        part = grad_conv[:, :span, :]
        weighted = weights[level_idx] * part
        carried = rounded(s_low * front_adjoint[:, :span, :] + s_high * weighted)
        fronts.append(carried[:, :spacing, :])
        if level_idx > 0:
            front_adjoint = (
                c_low * front_adjoint[:, :spacing, :]
                + c_high * weighted[:, :spacing, :]
                + carried[:, spacing:, :].astype(jnp.float32)
            )
    rims = shifted_2(jnp.concatenate(fronts, axis=1), "seq", -1)
    offset = 0
    for level_idx in reversed(range(near_count)):
        spacing = 2**level_idx
        current = states[level_idx].astype(jnp.float32)
        previous = shifted_states[level_idx].astype(jnp.float32)
        weighted = weights[level_idx] * grad_conv
        level_grads[level_idx] = jnp.sum(
            grad_conv * (c_high * current + s_high * previous), axis=(0, 1)
        )
        totals = tap_terms(totals, adjoint, weighted, current, previous)
        carried = rounded(s_low * adjoint + s_high * weighted)
        rim_rows = rims[:, offset : offset + spacing, :]
        offset += spacing
        arrived = jnp.concatenate([carried[:, spacing:, :], rim_rows], axis=1).astype(jnp.float32)
        adjoint = c_low * adjoint + c_high * weighted + arrived
    angle_terms = jnp.stack(
        [c_low * totals[1] - s_low * totals[0], c_high * totals[3] - s_high * totals[2]]
    )
    summed = butterfly_sum(jnp.concatenate([angle_terms, jnp.stack(level_grads)], axis=0), "seq")
    angle_total = summed[:2]
    level_total = summed[2:]
    grad_input = (received.astype(jnp.float32) + adjoint).astype(jnp.bfloat16)
    return (
        grad_input[None],
        (angle_total * grad_scale)[None],
        (level_total * grad_scale)[None],
        grad_weight[None],
    )


def solution(mesh):
    placed = (
        P("pipe", None, "seq", None),
        P("pipe", None, "seq", None),
        P("pipe", None, None),
        P("pipe", None, None),
        P("pipe", None, None),
    )
    return jax.shard_map(
        shards,
        mesh=mesh,
        in_specs=placed,
        out_specs=(
            P("pipe", None, "seq", None),
            P("pipe", None, None),
            P("pipe", None, None),
            P("pipe", "seq", None),
        ),
        check_vma=False,
    )
```

```python
import jax
import jax.numpy as jnp
from jax import lax
from jax.sharding import PartitionSpec as P


def shifted_3(value, axis, steps):
    count = lax.axis_size(axis)
    pairs = [(source, (source + steps) % count) for source in range(count)]
    return lax.ppermute(value, axis, pairs)


def rounded(values):
    return lax.optimization_barrier(values.astype(jnp.bfloat16))


def behind(values, spacing):
    return jnp.pad(values, ((0, 0), (0, 0), (spacing, 0)))[:, :, : values.shape[2]]


def from_later(values, spacing):
    return jnp.pad(values, ((0, 0), (0, 0), (0, spacing)))[:, :, spacing:]


def butterfly_sum(value, axis):
    count = lax.axis_size(axis)
    if count & (count - 1):
        return lax.psum(value, axis)
    step = 1
    while step < count:
        pairs = [(i, i ^ step) for i in range(count)]
        value = value + lax.ppermute(value, axis, pairs)
        step *= 2
    return value


def to_channels(block):
    gathered = lax.all_to_all(block, "seq", 2, 1, tiled=True)
    return jnp.transpose(gathered, (0, 2, 1))


def to_positions(block):
    return lax.all_to_all(jnp.transpose(block, (0, 2, 1)), "seq", 1, 2, tiled=True)


def shards(inputs, incoming, angles, level_weights, mix_weight):
    sequences, positions, channels = inputs.shape[1:]
    seq_devices = lax.axis_size("seq")
    width = channels // seq_devices
    total = positions * seq_devices
    levels = level_weights.shape[1] - 1
    grad_scale = float(sequences * total) ** (-0.5)
    me = lax.axis_index("seq")
    w_mix = mix_weight[0]
    own_angles = lax.dynamic_slice_in_dim(angles[0], me * width, width, axis=1)[:, :, None]
    weights = lax.dynamic_slice_in_dim(level_weights[0], me * width, width, axis=1)[:, :, None]
    c_low = jnp.cos(own_angles[0])
    s_low = jnp.sin(own_angles[0])
    c_high = jnp.cos(own_angles[1])
    s_high = jnp.sin(own_angles[1])
    received = shifted_3(incoming, "pipe", -1)[0]
    state_now = to_channels(inputs[0])
    states = []
    mixed = jnp.zeros(state_now.shape, jnp.float32)
    for level_idx in range(levels):
        spacing = 2**level_idx
        current = state_now.astype(jnp.float32)
        previous = behind(current, spacing)
        mixed = mixed + weights[level_idx] * (c_high * current + s_high * previous)
        states.append(state_now)
        state_now = rounded(c_low * current + s_low * previous)
    top_state = state_now.astype(jnp.float32)
    mixed = mixed + weights[levels] * top_state
    activated_local = jax.nn.gelu(mixed).astype(jnp.bfloat16)
    activated = to_positions(activated_local).reshape(-1, channels)
    projected = jnp.dot(activated, w_mix, preferred_element_type=jnp.float32)
    value_half = projected[:, :channels]
    gate_value = jax.nn.sigmoid(projected[:, channels:])
    upstream = received.reshape(-1, channels).astype(jnp.float32)
    grad_proj = jnp.concatenate(
        [upstream * gate_value, upstream * value_half * gate_value * (1.0 - gate_value)], axis=1
    ).astype(jnp.bfloat16)
    grad_act = jnp.einsum("rk,ck->rc", grad_proj, w_mix, preferred_element_type=jnp.float32)
    grad_weight = (
        lax.psum_scatter(
            jnp.einsum("rc,rk->ck", activated, grad_proj, preferred_element_type=jnp.float32),
            "seq",
            scatter_dimension=0,
            tiled=True,
        )
        * grad_scale
    )
    grad_act_local = to_channels(grad_act.reshape(sequences, positions, channels))
    _, pullback = jax.vjp(jax.nn.gelu, mixed)
    grad_conv = pullback(grad_act_local)[0]
    level_grads = [None] * (levels + 1)
    adjoint = weights[levels] * grad_conv
    level_grads[levels] = jnp.sum(grad_conv * top_state, axis=(0, 2))
    zero_row = jnp.zeros((width,), jnp.float32)
    tap_low_now, tap_low_back, tap_high_now, tap_high_back = (zero_row,) * 4
    for level_idx in reversed(range(levels)):
        spacing = 2**level_idx
        current = states[level_idx].astype(jnp.float32)
        previous = behind(current, spacing)
        weighted = weights[level_idx] * grad_conv
        level_grads[level_idx] = jnp.sum(
            grad_conv * (c_high * current + s_high * previous), axis=(0, 2)
        )
        tap_low_now = tap_low_now + jnp.sum(adjoint * current, axis=(0, 2))
        tap_low_back = tap_low_back + jnp.sum(adjoint * previous, axis=(0, 2))
        tap_high_now = tap_high_now + jnp.sum(weighted * current, axis=(0, 2))
        tap_high_back = tap_high_back + jnp.sum(weighted * previous, axis=(0, 2))
        carried = rounded(s_low * adjoint + s_high * weighted).astype(jnp.float32)
        adjoint = c_low * adjoint + c_high * weighted + from_later(carried, spacing)
    angle_terms = jnp.stack(
        [
            c_low[:, 0] * tap_low_back - s_low[:, 0] * tap_low_now,
            c_high[:, 0] * tap_high_back - s_high[:, 0] * tap_high_now,
        ]
    )
    small = jnp.concatenate([angle_terms, jnp.stack(level_grads)], axis=0)
    placed = lax.dynamic_update_slice_in_dim(
        jnp.zeros((small.shape[0], channels), jnp.float32), small, me * width, axis=1
    )
    summed = butterfly_sum(placed, "seq")
    adjoint_rows = to_positions(adjoint)
    grad_input = (received.astype(jnp.float32) + adjoint_rows).astype(jnp.bfloat16)
    return (
        grad_input[None],
        (summed[:2] * grad_scale)[None],
        (summed[2:] * grad_scale)[None],
        grad_weight[None],
    )


def solution(mesh):
    placed = (
        P("pipe", None, "seq", None),
        P("pipe", None, "seq", None),
        P("pipe", None, None),
        P("pipe", None, None),
        P("pipe", None, None),
    )
    return jax.shard_map(
        shards,
        mesh=mesh,
        in_specs=placed,
        out_specs=(
            P("pipe", None, "seq", None),
            P("pipe", None, None),
            P("pipe", None, None),
            P("pipe", "seq", None),
        ),
        check_vma=False,
    )
```

```python
import jax
import jax.numpy as jnp
from jax import lax
from jax.sharding import PartitionSpec as P


def shifted_3(value, axis, steps):
    count = lax.axis_size(axis)
    pairs = [(source, (source + steps) % count) for source in range(count)]
    return lax.ppermute(value, axis, pairs)


def rounded(values):
    return lax.optimization_barrier(values.astype(jnp.bfloat16))


def behind(values, spacing):
    rows = values.shape[-1]
    if spacing % rows == 0:
        step = spacing // rows
        return jnp.concatenate([jnp.zeros_like(values[:step]), values[:-step]], axis=0)
    prior = jnp.concatenate([jnp.zeros_like(values[:1]), values[:-1]], axis=0)
    return jnp.concatenate([prior[..., rows - spacing :], values[..., : rows - spacing]], axis=-1)


def from_later(values, spacing):
    rows = values.shape[-1]
    if spacing % rows == 0:
        step = spacing // rows
        return jnp.concatenate([values[step:], jnp.zeros_like(values[:step])], axis=0)
    later = jnp.concatenate([values[1:], jnp.zeros_like(values[:1])], axis=0)
    return jnp.concatenate([values[..., spacing:], later[..., :spacing]], axis=-1)


def to_channels(block, groups):
    sequences, rows, channels = block.shape
    flipped = jnp.swapaxes(block, 1, 2).reshape(sequences, groups, channels // groups, rows)
    return lax.all_to_all(jnp.transpose(flipped, (1, 0, 2, 3)), "seq", 0, 0, tiled=True)


def from_channels(block):
    groups, sequences, width, rows = block.shape
    flipped = jnp.transpose(block, (1, 0, 2, 3)).reshape(sequences, groups * width, rows)
    return jnp.swapaxes(flipped, 1, 2)


def shards(inputs, incoming, angles, level_weights, mix_weight):
    sequences, positions, channels = inputs.shape[1:]
    seq_devices = lax.axis_size("seq")
    width = channels // seq_devices
    total = positions * seq_devices
    levels = level_weights.shape[1] - 1
    grad_scale = float(sequences * total) ** (-0.5)
    me = lax.axis_index("seq")
    w_mix = mix_weight[0]
    own_angles = lax.dynamic_slice_in_dim(angles[0], me * width, width, axis=1)[:, :, None]
    weights = lax.dynamic_slice_in_dim(level_weights[0], me * width, width, axis=1)[:, :, None]
    c_low = jnp.cos(own_angles[0])
    s_low = jnp.sin(own_angles[0])
    c_high = jnp.cos(own_angles[1])
    s_high = jnp.sin(own_angles[1])
    received = shifted_3(incoming, "pipe", -1)[0]
    state_now = to_channels(inputs[0], seq_devices)
    states = []
    mixed = jnp.zeros(state_now.shape, jnp.float32)
    for level_idx in range(levels):
        spacing = 2**level_idx
        current = state_now.astype(jnp.float32)
        previous = behind(current, spacing)
        mixed = mixed + weights[level_idx] * (c_high * current + s_high * previous)
        states.append(state_now)
        state_now = rounded(c_low * current + s_low * previous)
    top_state = state_now.astype(jnp.float32)
    mixed = mixed + weights[levels] * top_state
    activated_local = jax.nn.gelu(mixed).astype(jnp.bfloat16)
    activated = from_channels(lax.all_to_all(activated_local, "seq", 0, 0, tiled=True))
    activated = activated.reshape(-1, channels)
    projected = jnp.dot(activated, w_mix, preferred_element_type=jnp.float32)
    value_half = projected[:, :channels]
    gate_value = jax.nn.sigmoid(projected[:, channels:])
    upstream = received.reshape(-1, channels).astype(jnp.float32)
    grad_proj = jnp.concatenate(
        [upstream * gate_value, upstream * value_half * gate_value * (1.0 - gate_value)], axis=1
    ).astype(jnp.bfloat16)
    grad_act = jnp.einsum("rk,ck->rc", grad_proj, w_mix, preferred_element_type=jnp.float32)
    grad_weight = (
        lax.psum_scatter(
            jnp.einsum("rc,rk->ck", activated, grad_proj, preferred_element_type=jnp.float32),
            "seq",
            scatter_dimension=0,
            tiled=True,
        )
        * grad_scale
    )
    grad_act_local = to_channels(grad_act.reshape(sequences, positions, channels), seq_devices)
    _, pullback = jax.vjp(jax.nn.gelu, mixed)
    grad_conv = pullback(grad_act_local)[0]
    sum_axes = (0, 1, 3)
    level_grads = [None] * (levels + 1)
    adjoint = weights[levels] * grad_conv
    level_grads[levels] = jnp.sum(grad_conv * top_state, axis=sum_axes)
    zero_row = jnp.zeros((width,), jnp.float32)
    tap_low_now, tap_low_back, tap_high_now, tap_high_back = (zero_row,) * 4
    for level_idx in reversed(range(levels)):
        spacing = 2**level_idx
        current = states[level_idx].astype(jnp.float32)
        previous = behind(current, spacing)
        weighted = weights[level_idx] * grad_conv
        level_grads[level_idx] = jnp.sum(
            grad_conv * (c_high * current + s_high * previous), axis=sum_axes
        )
        tap_low_now = tap_low_now + jnp.sum(adjoint * current, axis=sum_axes)
        tap_low_back = tap_low_back + jnp.sum(adjoint * previous, axis=sum_axes)
        tap_high_now = tap_high_now + jnp.sum(weighted * current, axis=sum_axes)
        tap_high_back = tap_high_back + jnp.sum(weighted * previous, axis=sum_axes)
        carried = rounded(s_low * adjoint + s_high * weighted).astype(jnp.float32)
        adjoint = c_low * adjoint + c_high * weighted + from_later(carried, spacing)
    angle_terms = jnp.stack(
        [
            c_low[:, 0] * tap_low_back - s_low[:, 0] * tap_low_now,
            c_high[:, 0] * tap_high_back - s_high[:, 0] * tap_high_now,
        ]
    )
    small = jnp.concatenate([angle_terms, jnp.stack(level_grads)], axis=0)
    rows_small = small.shape[0]
    plane = jnp.pad(small.T, ((0, 0), (0, positions - rows_small)))
    plane = jnp.broadcast_to(plane[None, None], (seq_devices, 1, width, positions))
    exchanged = lax.all_to_all(
        jnp.concatenate([adjoint, plane], axis=1), "seq", 0, 0, tiled=True
    )
    adjoint_rows = from_channels(exchanged[:, :sequences])
    gathered = exchanged[:, sequences, :, :rows_small]
    summed = jnp.transpose(gathered, (2, 0, 1)).reshape(rows_small, channels)
    grad_input = (received.astype(jnp.float32) + adjoint_rows).astype(jnp.bfloat16)
    return (
        grad_input[None],
        (summed[:2] * grad_scale)[None],
        (summed[2:] * grad_scale)[None],
        grad_weight[None],
    )


def solution(mesh):
    placed = (
        P("pipe", None, "seq", None),
        P("pipe", None, "seq", None),
        P("pipe", None, None),
        P("pipe", None, None),
        P("pipe", None, None),
    )
    return jax.shard_map(
        shards,
        mesh=mesh,
        in_specs=placed,
        out_specs=(
            P("pipe", None, "seq", None),
            P("pipe", None, None),
            P("pipe", None, None),
            P("pipe", "seq", None),
        ),
        check_vma=False,
    )
```

```python
import jax
import jax.numpy as jnp
from jax import lax
from jax.sharding import PartitionSpec as P


def shifted_3(value, axis, steps):
    count = lax.axis_size(axis)
    pairs = [(source, (source + steps) % count) for source in range(count)]
    return lax.ppermute(value, axis, pairs)


def rounded(values):
    return lax.optimization_barrier(values.astype(jnp.bfloat16))


def behind(values, spacing):
    rows = values.shape[-1]
    if spacing % rows == 0:
        step = spacing // rows
        return jnp.concatenate([jnp.zeros_like(values[:step]), values[:-step]], axis=0)
    prior = jnp.concatenate([jnp.zeros_like(values[:1]), values[:-1]], axis=0)
    return jnp.concatenate([prior[..., rows - spacing :], values[..., : rows - spacing]], axis=-1)


def from_later(values, spacing):
    rows = values.shape[-1]
    if spacing % rows == 0:
        step = spacing // rows
        return jnp.concatenate([values[step:], jnp.zeros_like(values[:step])], axis=0)
    later = jnp.concatenate([values[1:], jnp.zeros_like(values[:1])], axis=0)
    return jnp.concatenate([values[..., spacing:], later[..., :spacing]], axis=-1)


def to_channels(block, groups):
    sequences, rows, channels = block.shape
    flipped = jnp.swapaxes(block, 1, 2).reshape(sequences, groups, channels // groups, rows)
    return lax.all_to_all(jnp.transpose(flipped, (1, 0, 2, 3)), "seq", 0, 0, tiled=True)


def from_channels(block):
    groups, sequences, width, rows = block.shape
    flipped = jnp.transpose(block, (1, 0, 2, 3)).reshape(sequences, groups * width, rows)
    return jnp.swapaxes(flipped, 1, 2)


def body(inputs, incoming, angles, level_weights, mix_weight):
    sequences, positions, channels = inputs.shape[1:]
    seq_devices = lax.axis_size("seq")
    width = channels // seq_devices
    total = positions * seq_devices
    levels = level_weights.shape[1] - 1
    grad_scale = float(sequences * total) ** (-0.5)
    me = lax.axis_index("seq")
    w_mix = mix_weight[0]
    own_angles = lax.dynamic_slice_in_dim(angles[0], me * width, width, axis=1)[:, :, None]
    weights = lax.dynamic_slice_in_dim(level_weights[0], me * width, width, axis=1)[:, :, None]
    c_low = jnp.cos(own_angles[0])
    s_low = jnp.sin(own_angles[0])
    c_high = jnp.cos(own_angles[1])
    s_high = jnp.sin(own_angles[1])
    received = shifted_3(incoming, "pipe", -1)[0]
    state_now = to_channels(inputs[0], seq_devices)
    states = []
    mixed = jnp.zeros(state_now.shape, jnp.float32)
    for level_idx in range(levels):
        spacing = 2**level_idx
        current = state_now.astype(jnp.float32)
        previous = behind(current, spacing)
        mixed = mixed + weights[level_idx] * (c_high * current + s_high * previous)
        states.append(state_now)
        state_now = rounded(c_low * current + s_low * previous)
    top_state = state_now.astype(jnp.float32)
    mixed = mixed + weights[levels] * top_state
    activated_local = jax.nn.gelu(mixed).astype(jnp.bfloat16)
    activated = from_channels(lax.all_to_all(activated_local, "seq", 0, 0, tiled=True))
    activated = activated.reshape(-1, channels)
    projected = jnp.dot(activated, w_mix, preferred_element_type=jnp.float32)
    value_half = projected[:, :channels]
    gate_value = jax.nn.sigmoid(projected[:, channels:])
    upstream = received.reshape(-1, channels).astype(jnp.float32)
    grad_proj = jnp.concatenate(
        [upstream * gate_value, upstream * value_half * gate_value * (1.0 - gate_value)], axis=1
    ).astype(jnp.bfloat16)
    grad_act = jnp.einsum("rk,ck->rc", grad_proj, w_mix, preferred_element_type=jnp.float32)
    partial = jnp.einsum("rc,rk->ck", activated, grad_proj, preferred_element_type=jnp.float32)
    pieces = lax.all_to_all(
        partial.astype(jnp.bfloat16).reshape(seq_devices, width, 2 * channels),
        "seq",
        0,
        0,
        tiled=True,
    )
    grad_weight = jnp.sum(pieces.astype(jnp.float32), axis=0) * grad_scale
    grad_act_local = to_channels(grad_act.reshape(sequences, positions, channels), seq_devices)
    _, pullback = jax.vjp(jax.nn.gelu, mixed)
    grad_conv = pullback(grad_act_local)[0]
    sum_axes = (0, 1, 3)
    level_grads = [None] * (levels + 1)
    adjoint = weights[levels] * grad_conv
    level_grads[levels] = jnp.sum(grad_conv * top_state, axis=sum_axes)
    zero_row = jnp.zeros((width,), jnp.float32)
    tap_low_now, tap_low_back, tap_high_now, tap_high_back = (zero_row,) * 4
    for level_idx in reversed(range(levels)):
        spacing = 2**level_idx
        current = states[level_idx].astype(jnp.float32)
        previous = behind(current, spacing)
        weighted = weights[level_idx] * grad_conv
        level_grads[level_idx] = jnp.sum(
            grad_conv * (c_high * current + s_high * previous), axis=sum_axes
        )
        tap_low_now = tap_low_now + jnp.sum(adjoint * current, axis=sum_axes)
        tap_low_back = tap_low_back + jnp.sum(adjoint * previous, axis=sum_axes)
        tap_high_now = tap_high_now + jnp.sum(weighted * current, axis=sum_axes)
        tap_high_back = tap_high_back + jnp.sum(weighted * previous, axis=sum_axes)
        carried = rounded(s_low * adjoint + s_high * weighted).astype(jnp.float32)
        adjoint = c_low * adjoint + c_high * weighted + from_later(carried, spacing)
    angle_terms = jnp.stack(
        [
            c_low[:, 0] * tap_low_back - s_low[:, 0] * tap_low_now,
            c_high[:, 0] * tap_high_back - s_high[:, 0] * tap_high_now,
        ]
    )
    small = jnp.concatenate([angle_terms, jnp.stack(level_grads)], axis=0)
    rows_small = small.shape[0]
    plane = jnp.pad(small.T, ((0, 0), (0, positions - rows_small)))
    plane = jnp.broadcast_to(plane[None, None], (seq_devices, 1, width, positions))
    exchanged = lax.all_to_all(jnp.concatenate([adjoint, plane], axis=1), "seq", 0, 0, tiled=True)
    adjoint_rows = from_channels(exchanged[:, :sequences])
    gathered = exchanged[:, sequences, :, :rows_small]
    summed = jnp.transpose(gathered, (2, 0, 1)).reshape(rows_small, channels)
    grad_input = (received.astype(jnp.float32) + adjoint_rows).astype(jnp.bfloat16)
    return (
        grad_input[None],
        (summed[:2] * grad_scale)[None],
        (summed[2:] * grad_scale)[None],
        grad_weight[None],
    )


def solution(mesh):
    placed = (
        P("pipe", None, "seq", None),
        P("pipe", None, "seq", None),
        P("pipe", None, None),
        P("pipe", None, None),
        P("pipe", None, None),
    )
    return jax.shard_map(
        body,
        mesh=mesh,
        in_specs=placed,
        out_specs=(
            P("pipe", None, "seq", None),
            P("pipe", None, None),
            P("pipe", None, None),
            P("pipe", "seq", None),
        ),
        check_vma=False,
    )
```

```python
import jax
import jax.numpy as jnp
from jax import lax
from jax.sharding import PartitionSpec as P


def shifted_3(value, axis, steps):
    count = lax.axis_size(axis)
    pairs = [(source, (source + steps) % count) for source in range(count)]
    return lax.ppermute(value, axis, pairs)


def rounded(values):
    return lax.optimization_barrier(values.astype(jnp.bfloat16))


def behind(values, spacing):
    rows = values.shape[-1]
    if spacing % rows == 0:
        step = spacing // rows
        return jnp.concatenate([jnp.zeros_like(values[:step]), values[:-step]], axis=0)
    prior = jnp.concatenate([jnp.zeros_like(values[:1]), values[:-1]], axis=0)
    return jnp.concatenate([prior[..., rows - spacing :], values[..., : rows - spacing]], axis=-1)


def from_later(values, spacing):
    rows = values.shape[-1]
    if spacing % rows == 0:
        step = spacing // rows
        return jnp.concatenate([values[step:], jnp.zeros_like(values[:step])], axis=0)
    later = jnp.concatenate([values[1:], jnp.zeros_like(values[:1])], axis=0)
    return jnp.concatenate([values[..., spacing:], later[..., :spacing]], axis=-1)


def halving_sum(partial, axis):
    count = lax.axis_size(axis)
    me = lax.axis_index(axis)
    rows, cols = partial.shape
    buffer = partial.reshape(count, rows // count, cols)
    step = 1
    while step < count:
        split = buffer.reshape(buffer.shape[0] // 2, 2, rows // count, cols)
        mine = (me // step) % 2
        keep = lax.dynamic_index_in_dim(split, mine, axis=1, keepdims=False)
        send = lax.dynamic_index_in_dim(split, 1 - mine, axis=1, keepdims=False)
        pairs = [(i, i ^ step) for i in range(count)]
        arrived = lax.ppermute(send.astype(jnp.bfloat16), axis, pairs)
        buffer = keep + arrived.astype(jnp.float32)
        step *= 2
    return buffer[0]


def to_channels(block, groups):
    sequences, rows, channels = block.shape
    flipped = jnp.swapaxes(block, 1, 2).reshape(sequences, groups, channels // groups, rows)
    return lax.all_to_all(jnp.transpose(flipped, (1, 0, 2, 3)), "seq", 0, 0, tiled=True)


def from_channels(block):
    groups, sequences, width, rows = block.shape
    flipped = jnp.transpose(block, (1, 0, 2, 3)).reshape(sequences, groups * width, rows)
    return jnp.swapaxes(flipped, 1, 2)


def body(inputs, incoming, angles, level_weights, mix_weight):
    sequences, positions, channels = inputs.shape[1:]
    seq_devices = lax.axis_size("seq")
    width = channels // seq_devices
    total = positions * seq_devices
    levels = level_weights.shape[1] - 1
    grad_scale = float(sequences * total) ** (-0.5)
    me = lax.axis_index("seq")
    w_mix = mix_weight[0]
    own_angles = lax.dynamic_slice_in_dim(angles[0], me * width, width, axis=1)[:, :, None]
    weights = lax.dynamic_slice_in_dim(level_weights[0], me * width, width, axis=1)[:, :, None]
    c_low = jnp.cos(own_angles[0])
    s_low = jnp.sin(own_angles[0])
    c_high = jnp.cos(own_angles[1])
    s_high = jnp.sin(own_angles[1])
    received = shifted_3(incoming, "pipe", -1)[0]
    state_now = to_channels(inputs[0], seq_devices)
    states = []
    mixed = jnp.zeros(state_now.shape, jnp.float32)
    for level_idx in range(levels):
        spacing = 2**level_idx
        current = state_now.astype(jnp.float32)
        previous = behind(current, spacing)
        mixed = mixed + weights[level_idx] * (c_high * current + s_high * previous)
        states.append(state_now)
        state_now = rounded(c_low * current + s_low * previous)
    top_state = state_now.astype(jnp.float32)
    mixed = mixed + weights[levels] * top_state
    activated_local = jax.nn.gelu(mixed).astype(jnp.bfloat16)
    activated = from_channels(lax.all_to_all(activated_local, "seq", 0, 0, tiled=True))
    activated = activated.reshape(-1, channels)
    projected = jnp.dot(activated, w_mix, preferred_element_type=jnp.float32)
    value_half = projected[:, :channels]
    gate_value = jax.nn.sigmoid(projected[:, channels:])
    upstream = received.reshape(-1, channels).astype(jnp.float32)
    grad_proj = jnp.concatenate(
        [upstream * gate_value, upstream * value_half * gate_value * (1.0 - gate_value)], axis=1
    ).astype(jnp.bfloat16)
    grad_act = jnp.einsum("rk,ck->rc", grad_proj, w_mix, preferred_element_type=jnp.float32)
    partial = jnp.einsum("rc,rk->ck", activated, grad_proj, preferred_element_type=jnp.float32)
    grad_weight = halving_sum(partial, "seq") * grad_scale
    grad_act_local = to_channels(
        grad_act.astype(jnp.bfloat16).reshape(sequences, positions, channels), seq_devices
    ).astype(jnp.float32)
    _, pullback = jax.vjp(jax.nn.gelu, mixed)
    grad_conv = pullback(grad_act_local)[0]
    sum_axes = (0, 1, 3)
    level_grads = [None] * (levels + 1)
    adjoint = weights[levels] * grad_conv
    level_grads[levels] = jnp.sum(grad_conv * top_state, axis=sum_axes)
    zero_row = jnp.zeros((width,), jnp.float32)
    tap_low_now, tap_low_back, tap_high_now, tap_high_back = (zero_row,) * 4
    for level_idx in reversed(range(levels)):
        spacing = 2**level_idx
        current = states[level_idx].astype(jnp.float32)
        previous = behind(current, spacing)
        weighted = weights[level_idx] * grad_conv
        level_grads[level_idx] = jnp.sum(
            grad_conv * (c_high * current + s_high * previous), axis=sum_axes
        )
        tap_low_now = tap_low_now + jnp.sum(adjoint * current, axis=sum_axes)
        tap_low_back = tap_low_back + jnp.sum(adjoint * previous, axis=sum_axes)
        tap_high_now = tap_high_now + jnp.sum(weighted * current, axis=sum_axes)
        tap_high_back = tap_high_back + jnp.sum(weighted * previous, axis=sum_axes)
        carried = rounded(s_low * adjoint + s_high * weighted).astype(jnp.float32)
        adjoint = c_low * adjoint + c_high * weighted + from_later(carried, spacing)
    angle_terms = jnp.stack(
        [
            c_low[:, 0] * tap_low_back - s_low[:, 0] * tap_low_now,
            c_high[:, 0] * tap_high_back - s_high[:, 0] * tap_high_now,
        ]
    )
    small = jnp.concatenate([angle_terms, jnp.stack(level_grads)], axis=0)
    rows_small = small.shape[0]
    plane = jnp.pad(small.T, ((0, 0), (0, positions - rows_small)))
    plane = jnp.broadcast_to(plane[None, None], (seq_devices, 1, width, positions))
    exchanged = lax.all_to_all(jnp.concatenate([adjoint, plane], axis=1), "seq", 0, 0, tiled=True)
    adjoint_rows = from_channels(exchanged[:, :sequences])
    gathered = exchanged[:, sequences, :, :rows_small]
    summed = jnp.transpose(gathered, (2, 0, 1)).reshape(rows_small, channels)
    grad_input = (received.astype(jnp.float32) + adjoint_rows).astype(jnp.bfloat16)
    return (
        grad_input[None],
        (summed[:2] * grad_scale)[None],
        (summed[2:] * grad_scale)[None],
        grad_weight[None],
    )


def solution(mesh):
    placed = (
        P("pipe", None, "seq", None),
        P("pipe", None, "seq", None),
        P("pipe", None, None),
        P("pipe", None, None),
        P("pipe", None, None),
    )
    return jax.shard_map(
        body,
        mesh=mesh,
        in_specs=placed,
        out_specs=(
            P("pipe", None, "seq", None),
            P("pipe", None, None),
            P("pipe", None, None),
            P("pipe", "seq", None),
        ),
        check_vma=False,
    )
```

```python
import jax
import jax.numpy as jnp
from jax import lax
from jax.sharding import PartitionSpec as P


def shifted_3(value, axis, steps):
    count = lax.axis_size(axis)
    pairs = [(source, (source + steps) % count) for source in range(count)]
    return lax.ppermute(value, axis, pairs)


def rounded(values):
    return lax.optimization_barrier(values.astype(jnp.bfloat16))


def behind(values, spacing):
    rows = values.shape[-1]
    if spacing % rows == 0:
        step = spacing // rows
        return jnp.concatenate([jnp.zeros_like(values[:step]), values[:-step]], axis=0)
    prior = jnp.concatenate([jnp.zeros_like(values[:1]), values[:-1]], axis=0)
    return jnp.concatenate([prior[..., rows - spacing :], values[..., : rows - spacing]], axis=-1)


def from_later(values, spacing):
    rows = values.shape[-1]
    if spacing % rows == 0:
        step = spacing // rows
        return jnp.concatenate([values[step:], jnp.zeros_like(values[:step])], axis=0)
    later = jnp.concatenate([values[1:], jnp.zeros_like(values[:1])], axis=0)
    return jnp.concatenate([values[..., spacing:], later[..., :spacing]], axis=-1)


def halving_sum(partial, axis):
    count = lax.axis_size(axis)
    me = lax.axis_index(axis)
    rows, cols = partial.shape
    bits = count.bit_length() - 1
    block = rows // count
    if bits < 2:
        orders = (tuple(range(bits)), tuple(range(bits)))
    else:
        rest = list(range(1, bits))
        low = [b for b in rest if b <= (bits - 1) // 2]
        high = [b for b in rest if b > (bits - 1) // 2]
        orders = (tuple([0] + low + high), tuple([0] + high + low))
    odd = (me % 2) == 1
    buffer = partial.reshape((2,) * bits + (block, cols))
    remaining = [list(range(bits - 1, -1, -1)), list(range(bits - 1, -1, -1))]
    for step in range(bits):
        halves = []
        for parity in range(2):
            bit = orders[parity][step]
            where = remaining[parity].index(bit)
            mine = (me >> bit) % 2
            keep = lax.dynamic_index_in_dim(buffer, mine, axis=where, keepdims=False)
            send = lax.dynamic_index_in_dim(buffer, 1 - mine, axis=where, keepdims=False)
            halves.append((keep, send))
            remaining[parity].remove(bit)
        if orders[0][step] == orders[1][step]:
            keep, send = halves[0]
        else:
            keep = jnp.where(odd, halves[1][0], halves[0][0])
            send = jnp.where(odd, halves[1][1], halves[0][1])
        pairs = [(i, i ^ (1 << orders[i % 2][step])) for i in range(count)]
        arrived = lax.ppermute(send.astype(jnp.bfloat16), axis, pairs)
        buffer = keep + arrived.astype(jnp.float32)
    return buffer.reshape(block, cols)


def to_channels(block, groups):
    sequences, rows, channels = block.shape
    flipped = jnp.swapaxes(block, 1, 2).reshape(sequences, groups, channels // groups, rows)
    return lax.all_to_all(jnp.transpose(flipped, (1, 0, 2, 3)), "seq", 0, 0, tiled=True)


def from_channels(block):
    groups, sequences, width, rows = block.shape
    flipped = jnp.transpose(block, (1, 0, 2, 3)).reshape(sequences, groups * width, rows)
    return jnp.swapaxes(flipped, 1, 2)


def body(inputs, incoming, angles, level_weights, mix_weight):
    sequences, positions, channels = inputs.shape[1:]
    seq_devices = lax.axis_size("seq")
    width = channels // seq_devices
    total = positions * seq_devices
    levels = level_weights.shape[1] - 1
    grad_scale = float(sequences * total) ** (-0.5)
    me = lax.axis_index("seq")
    w_mix = mix_weight[0]
    own_angles = lax.dynamic_slice_in_dim(angles[0], me * width, width, axis=1)[:, :, None]
    weights = lax.dynamic_slice_in_dim(level_weights[0], me * width, width, axis=1)[:, :, None]
    c_low = jnp.cos(own_angles[0])
    s_low = jnp.sin(own_angles[0])
    c_high = jnp.cos(own_angles[1])
    s_high = jnp.sin(own_angles[1])
    received = shifted_3(incoming, "pipe", -1)[0]
    state_now = to_channels(inputs[0], seq_devices)
    states = []
    mixed = jnp.zeros(state_now.shape, jnp.float32)
    for level_idx in range(levels):
        spacing = 2**level_idx
        current = state_now.astype(jnp.float32)
        previous = behind(current, spacing)
        mixed = mixed + weights[level_idx] * (c_high * current + s_high * previous)
        states.append(state_now)
        state_now = rounded(c_low * current + s_low * previous)
    top_state = state_now.astype(jnp.float32)
    mixed = mixed + weights[levels] * top_state
    activated_local = jax.nn.gelu(mixed).astype(jnp.bfloat16)
    activated = from_channels(lax.all_to_all(activated_local, "seq", 0, 0, tiled=True))
    activated = activated.reshape(-1, channels)
    projected = jnp.dot(activated, w_mix, preferred_element_type=jnp.float32)
    value_half = projected[:, :channels]
    gate_value = jax.nn.sigmoid(projected[:, channels:])
    upstream = received.reshape(-1, channels).astype(jnp.float32)
    grad_proj = jnp.concatenate(
        [upstream * gate_value, upstream * value_half * gate_value * (1.0 - gate_value)], axis=1
    ).astype(jnp.bfloat16)
    grad_act = jnp.einsum("rk,ck->rc", grad_proj, w_mix, preferred_element_type=jnp.float32)
    partial = jnp.einsum("rc,rk->ck", activated, grad_proj, preferred_element_type=jnp.float32)
    grad_weight = halving_sum(partial, "seq") * grad_scale
    grad_act_local = to_channels(
        grad_act.astype(jnp.bfloat16).reshape(sequences, positions, channels), seq_devices
    ).astype(jnp.float32)
    _, pullback = jax.vjp(jax.nn.gelu, mixed)
    grad_conv = pullback(grad_act_local)[0]
    sum_axes = (0, 1, 3)
    level_grads = [None] * (levels + 1)
    adjoint = weights[levels] * grad_conv
    level_grads[levels] = jnp.sum(grad_conv * top_state, axis=sum_axes)
    zero_row = jnp.zeros((width,), jnp.float32)
    tap_low_now, tap_low_back, tap_high_now, tap_high_back = (zero_row,) * 4
    for level_idx in reversed(range(levels)):
        spacing = 2**level_idx
        current = states[level_idx].astype(jnp.float32)
        previous = behind(current, spacing)
        weighted = weights[level_idx] * grad_conv
        level_grads[level_idx] = jnp.sum(
            grad_conv * (c_high * current + s_high * previous), axis=sum_axes
        )
        tap_low_now = tap_low_now + jnp.sum(adjoint * current, axis=sum_axes)
        tap_low_back = tap_low_back + jnp.sum(adjoint * previous, axis=sum_axes)
        tap_high_now = tap_high_now + jnp.sum(weighted * current, axis=sum_axes)
        tap_high_back = tap_high_back + jnp.sum(weighted * previous, axis=sum_axes)
        carried = rounded(s_low * adjoint + s_high * weighted).astype(jnp.float32)
        adjoint = c_low * adjoint + c_high * weighted + from_later(carried, spacing)
    angle_terms = jnp.stack(
        [
            c_low[:, 0] * tap_low_back - s_low[:, 0] * tap_low_now,
            c_high[:, 0] * tap_high_back - s_high[:, 0] * tap_high_now,
        ]
    )
    small = jnp.concatenate([angle_terms, jnp.stack(level_grads)], axis=0)
    rows_small = small.shape[0]
    plane = jnp.pad(small.T, ((0, 0), (0, positions - rows_small)))
    plane = jnp.broadcast_to(plane[None, None], (seq_devices, 1, width, positions))
    exchanged = lax.all_to_all(jnp.concatenate([adjoint, plane], axis=1), "seq", 0, 0, tiled=True)
    adjoint_rows = from_channels(exchanged[:, :sequences])
    gathered = exchanged[:, sequences, :, :rows_small]
    summed = jnp.transpose(gathered, (2, 0, 1)).reshape(rows_small, channels)
    grad_input = (received.astype(jnp.float32) + adjoint_rows).astype(jnp.bfloat16)
    return (
        grad_input[None],
        (summed[:2] * grad_scale)[None],
        (summed[2:] * grad_scale)[None],
        grad_weight[None],
    )


def solution(mesh):
    placed = (
        P("pipe", None, "seq", None),
        P("pipe", None, "seq", None),
        P("pipe", None, None),
        P("pipe", None, None),
        P("pipe", None, None),
    )
    return jax.shard_map(
        body,
        mesh=mesh,
        in_specs=placed,
        out_specs=(
            P("pipe", None, "seq", None),
            P("pipe", None, None),
            P("pipe", None, None),
            P("pipe", "seq", None),
        ),
        check_vma=False,
    )
```

```python
import jax
import jax.numpy as jnp
from jax import lax
from jax.sharding import PartitionSpec as P


def shifted_3(value, axis, steps):
    count = lax.axis_size(axis)
    pairs = [(source, (source + steps) % count) for source in range(count)]
    return lax.ppermute(value, axis, pairs)


def rounded(values):
    return lax.optimization_barrier(values.astype(jnp.bfloat16))


def behind(values, spacing):
    rows = values.shape[-1]
    if spacing % rows == 0:
        step = spacing // rows
        return jnp.concatenate([jnp.zeros_like(values[:step]), values[:-step]], axis=0)
    prior = jnp.concatenate([jnp.zeros_like(values[:1]), values[:-1]], axis=0)
    return jnp.concatenate([prior[..., rows - spacing :], values[..., : rows - spacing]], axis=-1)


def from_later(values, spacing):
    rows = values.shape[-1]
    if spacing % rows == 0:
        step = spacing // rows
        return jnp.concatenate([values[step:], jnp.zeros_like(values[:step])], axis=0)
    later = jnp.concatenate([values[1:], jnp.zeros_like(values[:1])], axis=0)
    return jnp.concatenate([values[..., spacing:], later[..., :spacing]], axis=-1)


def halving_sum(partial, axis):
    count = lax.axis_size(axis)
    me = lax.axis_index(axis)
    rows, cols = partial.shape
    buffer = partial.reshape(count, rows // count, cols)
    step = 1
    while step < count:
        split = buffer.reshape(buffer.shape[0] // 2, 2, rows // count, cols)
        mine = (me // step) % 2
        keep = lax.dynamic_index_in_dim(split, mine, axis=1, keepdims=False)
        send = lax.dynamic_index_in_dim(split, 1 - mine, axis=1, keepdims=False)
        pairs = [(i, i ^ step) for i in range(count)]
        arrived = lax.ppermute(send.astype(jnp.bfloat16), axis, pairs)
        buffer = keep + arrived.astype(jnp.float32)
        step *= 2
    return buffer[0]


def to_channels(block, groups):
    sequences, rows, channels = block.shape
    flipped = jnp.swapaxes(block, 1, 2).reshape(sequences, groups, channels // groups, rows)
    return lax.all_to_all(jnp.transpose(flipped, (1, 0, 2, 3)), "seq", 0, 0, tiled=True)


def from_channels(block):
    groups, sequences, width, rows = block.shape
    flipped = jnp.transpose(block, (1, 0, 2, 3)).reshape(sequences, groups * width, rows)
    return jnp.swapaxes(flipped, 1, 2)


def body(inputs, incoming, angles, level_weights, mix_weight):
    sequences, positions, channels = inputs.shape[1:]
    seq_devices = lax.axis_size("seq")
    width = channels // seq_devices
    total = positions * seq_devices
    levels = level_weights.shape[1] - 1
    grad_scale = float(sequences * total) ** (-0.5)
    me = lax.axis_index("seq")
    w_mix = mix_weight[0]
    own_angles = lax.dynamic_slice_in_dim(angles[0], me * width, width, axis=1)[:, :, None]
    weights = lax.dynamic_slice_in_dim(level_weights[0], me * width, width, axis=1)[:, :, None]
    c_low = jnp.cos(own_angles[0])
    s_low = jnp.sin(own_angles[0])
    c_high = jnp.cos(own_angles[1])
    s_high = jnp.sin(own_angles[1])
    received = shifted_3(incoming, "pipe", -1)[0]
    state_now = to_channels(inputs[0], seq_devices)
    states = []
    mixed = jnp.zeros(state_now.shape, jnp.float32)
    for level_idx in range(levels):
        spacing = 2**level_idx
        current = state_now.astype(jnp.float32)
        previous = behind(current, spacing)
        mixed = mixed + weights[level_idx] * (c_high * current + s_high * previous)
        states.append(state_now)
        state_now = rounded(c_low * current + s_low * previous)
    top_state = state_now.astype(jnp.float32)
    mixed = mixed + weights[levels] * top_state
    activated_local = jax.nn.gelu(mixed).astype(jnp.bfloat16)
    activated = from_channels(lax.all_to_all(activated_local, "seq", 0, 0, tiled=True))
    activated = activated.reshape(-1, channels)
    projected = jnp.dot(activated, w_mix, preferred_element_type=jnp.float32)
    value_half = projected[:, :channels]
    gate_value = jax.nn.sigmoid(projected[:, channels:])
    upstream = received.reshape(-1, channels).astype(jnp.float32)
    grad_proj = jnp.concatenate(
        [upstream * gate_value, upstream * value_half * gate_value * (1.0 - gate_value)], axis=1
    ).astype(jnp.bfloat16)
    grad_act = jnp.einsum("rk,ck->rc", grad_proj, w_mix, preferred_element_type=jnp.float32)
    partial = jnp.einsum("rc,rk->ck", activated, grad_proj, preferred_element_type=jnp.float32)
    grad_weight = halving_sum(partial, "seq") * grad_scale
    grad_act_local = to_channels(
        grad_act.astype(jnp.bfloat16).reshape(sequences, positions, channels), seq_devices
    ).astype(jnp.float32)
    _, pullback = jax.vjp(jax.nn.gelu, mixed)
    grad_conv = pullback(grad_act_local)[0]
    sum_axes = (0, 1)
    level_parts = [None] * (levels + 1)
    adjoint = weights[levels] * grad_conv
    level_parts[levels] = jnp.sum(grad_conv * top_state, axis=sum_axes)
    zero_part = jnp.zeros((width, positions), jnp.float32)
    low_now, low_back, high_now, high_back = (zero_part,) * 4
    for level_idx in reversed(range(levels)):
        spacing = 2**level_idx
        current = states[level_idx].astype(jnp.float32)
        previous = behind(current, spacing)
        weighted = weights[level_idx] * grad_conv
        with_now = jnp.sum(grad_conv * current, axis=sum_axes)
        with_back = jnp.sum(grad_conv * previous, axis=sum_axes)
        level_parts[level_idx] = c_high * with_now + s_high * with_back
        high_now = high_now + weights[level_idx] * with_now
        high_back = high_back + weights[level_idx] * with_back
        low_now = low_now + jnp.sum(adjoint * current, axis=sum_axes)
        low_back = low_back + jnp.sum(adjoint * previous, axis=sum_axes)
        carried = rounded(s_low * adjoint + s_high * weighted).astype(jnp.float32)
        adjoint = c_low * adjoint + c_high * weighted + from_later(carried, spacing)
    tap_low_now, tap_low_back, tap_high_now, tap_high_back = (
        jnp.sum(part, axis=-1) for part in (low_now, low_back, high_now, high_back)
    )
    angle_terms = jnp.stack(
        [
            c_low[:, 0] * tap_low_back - s_low[:, 0] * tap_low_now,
            c_high[:, 0] * tap_high_back - s_high[:, 0] * tap_high_now,
        ]
    )
    level_grads = jnp.sum(jnp.stack(level_parts), axis=-1)
    small = jnp.concatenate([angle_terms, level_grads], axis=0)
    rows_small = small.shape[0]
    flat = small.T.reshape(-1)
    extra = -(-flat.shape[0] // positions)
    flat = jnp.pad(flat, (0, extra * positions - flat.shape[0])).reshape(extra, positions)
    stacked = adjoint.reshape(seq_devices, sequences * width, positions)
    payload = jnp.concatenate(
        [stacked, jnp.broadcast_to(flat[None], (seq_devices, extra, positions))], axis=1
    )
    exchanged = lax.all_to_all(payload, "seq", 0, 0, tiled=True)
    adjoint_rows = from_channels(
        exchanged[:, : sequences * width].reshape(seq_devices, sequences, width, positions)
    )
    gathered = exchanged[:, sequences * width :].reshape(seq_devices, -1)
    gathered = gathered[:, : width * rows_small].reshape(seq_devices, width, rows_small)
    summed = jnp.transpose(gathered, (2, 0, 1)).reshape(rows_small, channels)
    grad_input = (received.astype(jnp.float32) + adjoint_rows).astype(jnp.bfloat16)
    return (
        grad_input[None],
        (summed[:2] * grad_scale)[None],
        (summed[2:] * grad_scale)[None],
        grad_weight[None],
    )


def solution(mesh):
    placed = (
        P("pipe", None, "seq", None),
        P("pipe", None, "seq", None),
        P("pipe", None, None),
        P("pipe", None, None),
        P("pipe", None, None),
    )
    return jax.shard_map(
        body,
        mesh=mesh,
        in_specs=placed,
        out_specs=(
            P("pipe", None, "seq", None),
            P("pipe", None, None),
            P("pipe", None, None),
            P("pipe", "seq", None),
        ),
        check_vma=False,
    )
```
